256 devices in a mesh: row: 16 (over y, x_lo, core), col: 16 (over x_hi, z).
Axes of the slice: x: 4 (x_hi: 2, x_lo: 2; x = x_hi * 2 + x_lo), y: 4, z: 8, core: 2. Of those that a mesh axis runs over, the one named last changes fastest.
Arguments:
- w_cycle: float32 [2048, 16384], P('col', 'row'), may hold values from -0.125 to 0.125
- amps: float32 [32, 512, 2048], P('col', 'row'), may hold values from -18 to 18
- eps_occ: float32 [32], replicated, may hold values from -3 to -0.3
- eps_vir: float32 [512], replicated, may hold values from 0.3 to 3
- occ_map: int32 [4], replicated, may hold values from 0 to 31
- vir_perm: int32 [512], replicated, may hold values from 0 to 511, each once
Outputs:
- cycle: float32 [16384, 16384], P('row', 'col')
The draws below stay inside these ranges and needn't reach their ends.
Inputs may be any that keep to these rules, and one draw needn't show every extreme that they name: `occ_map`: each window index names one occupied orbital. `vir_perm`: each virtual orbital appears once.
All inputs are finite; a program needn't handle non-finite values.
Results may differ from the reference program's by a relative error of at most 0.000071.
Values sent between devices are 32-bit elements; how exact they have to be, the bound alone decides.
No kernel may reach another device: no remote copies, remote signals or barrier semaphores. Data moves between devices by JAX's collectives and lax.ppermute only.
A program may use at most 64 MiB of HBM per device.

```python
import jax
import jax.numpy as jnp
from jax import lax

OCC = 32
VIR = 512
KW = 4
CK = 2048
ORDER = 16384


def set_ends(array, own_key, smallest, high):
    spot = [jax.random.randint(jax.random.fold_in(own_key, axis), (), 0, length) for axis, length in enumerate(array.shape)]
    widest = array.shape.index(max(array.shape))
    neighbour = spot[:widest] + [(spot[widest] + 1) % array.shape[widest]] + spot[widest + 1:]
    return array.at[tuple(spot)].set(smallest).at[tuple(neighbour)].set(high)


def block_scale(stream_key, shape, pieces, least, largest):
    loudness = 1.0
    for axis_at, blocks in pieces:
        steps = jax.random.uniform(jax.random.fold_in(jax.random.fold_in(stream_key, 6), axis_at), (blocks,), jnp.float32, least / len(pieces), largest / len(pieces))
        loudness = loudness * jnp.repeat(jnp.exp(steps), shape[axis_at] // blocks).reshape((-1,) + (1,) * (len(shape) - 1 - axis_at))
    return loudness


def bell_draw(stream_key, shape, spread, reach, pieces=(), kind=jnp.bfloat16):
    drawn = spread * jax.random.normal(stream_key, shape, jnp.float32)
    if pieces:
        drawn = drawn * block_scale(stream_key, shape, pieces, -0.22, 0.18)
    return jnp.clip(drawn, -reach, reach).astype(kind)


def setup_inputs(seed: int = 0) -> dict:
    keys = jax.random.split(jax.random.key(seed), 7)
    return {
        "w_cycle": bell_draw(keys[0], (CK, ORDER), CK ** -0.5, 0.125, ((0, 16), (1, 16)), jnp.float32),
        "amps": bell_draw(keys[1], (OCC, VIR, CK), 3.0, 18.0, ((0, 16), (1, 16)), jnp.float32),
        "eps_occ": jnp.clip(jax.random.uniform(keys[2], (OCC,), jnp.float32, -3.0, -0.3), -3.0, -0.3),
        "eps_vir": jnp.clip(jax.random.uniform(keys[3], (VIR,), jnp.float32, 0.3, 3.0), 0.3, 3.0),
        "occ_map": set_ends(jax.random.randint(keys[4], (KW,), 0, OCC), jax.random.fold_in(keys[4], 1), 0, OCC - 1).astype(jnp.int32),
        "vir_perm": jax.random.permutation(keys[5], VIR).astype(jnp.int32),
    }


def reference(w_cycle, amps, eps_occ, eps_vir, occ_map, vir_perm):
    vir_energy = eps_vir[vir_perm]
    occ_energy = eps_occ[occ_map]
    pair_energy = (vir_energy[None, :] - occ_energy[:, None]).reshape(-1)
    denominator = pair_energy[None, None, :] + vir_energy[None, :, None] - eps_occ[:, None, None]
    scaled = amps / denominator
    columns = scaled.reshape(OCC * VIR, KW * VIR)
    return lax.dot_general(w_cycle, columns, (((0,), (1,)), ((), ())),
                           precision=lax.Precision.HIGHEST,
                           preferred_element_type=jnp.float32)
```

```python
import jax
import jax.numpy as jnp
from jax import lax
from jax.sharding import Mesh
from jax.sharding import PartitionSpec as P

ROW = ("y", "xlo", "core")
COL = ("xhi", "z")


def lookup(indices, table):
    onehot = (indices[:, None] == jnp.arange(table.shape[0], dtype=jnp.int32)[None, :]).astype(
        jnp.float32
    )
    return jnp.dot(
        onehot, table, precision=lax.Precision.HIGHEST, preferred_element_type=jnp.float32
    )


def body(w_cycle, amps, eps_occ, eps_vir, occ_map, vir_perm):
    nz = lax.axis_size("z")
    nxhi = lax.axis_size("xhi")
    z = lax.axis_index("z")
    xhi = lax.axis_index("xhi")
    col = xhi * nz + z
    row = (lax.axis_index("y") * lax.axis_size("xlo") + lax.axis_index("xlo")) * lax.axis_size(
        "core"
    ) + lax.axis_index("core")

    j_local, b_local, ck = amps.shape
    kw = occ_energy_count = occ_map.shape[0]
    del occ_energy_count
    blk = w_cycle.shape[0]

    vir_energy = lookup(vir_perm, eps_vir)
    occ_energy = lookup(occ_map, eps_occ)
    pair_energy = (vir_energy[None, :] - occ_energy[:, None]).reshape(-1)
    j_index = jnp.arange(j_local, dtype=jnp.int32) + col * j_local
    j_energy = lookup(j_index, eps_occ)
    b_energy = lax.dynamic_slice_in_dim(vir_energy, row * b_local, b_local)
    denominator = pair_energy[None, None, :] + b_energy[None, :, None] - j_energy[:, None, None]
    scaled = amps / denominator

    s5 = scaled.reshape(j_local, b_local, nxhi, nz, blk)
    s5 = jnp.where(xhi == 0, s5, s5[:, :, ::-1])
    s5 = jnp.roll(s5, -z, axis=3)
    s_perm = s5.transpose(0, 1, 3, 2, 4).reshape(j_local, b_local, ck)
    s_full = lax.all_gather(s_perm, ROW, axis=1, tiled=True)
    del kw

    w_other = lax.ppermute(w_cycle, "xhi", [(0, 1), (1, 0)])
    fwd = [(k, (k + 1) % nz) for k in range(nz)]
    bwd = [(k, (k - 1) % nz) for k in range(nz)]
    blocks = {0: [w_cycle, w_other]}
    f_own, f_oth = w_cycle, w_other
    b_own, b_oth = w_cycle, w_other
    half = nz // 2
    for s in range(1, half + 1):
        f_own = lax.ppermute(f_own, "z", fwd)
        b_oth = lax.ppermute(b_oth, "z", bwd)
        if s < half:
            f_oth = lax.ppermute(f_oth, "z", fwd)
            b_own = lax.ppermute(b_own, "z", bwd)
            blocks[nz - s] = [f_own, f_oth]
            blocks[s] = [b_own, b_oth]
        else:
            blocks[s] = [f_own, b_oth]
    w_full = jnp.concatenate([blocks[d][t] for d in range(nz) for t in range(nxhi)], axis=0)

    return lax.dot_general(
        w_full,
        s_full.reshape(j_local * s_full.shape[1], ck),
        (((0,), (1,)), ((), ())),
        precision=lax.Precision.HIGH,
        preferred_element_type=jnp.float32,
    )


def solution(mesh):
    nrow, ncol = mesh.devices.shape
    ncore = 2
    nxlo = 2
    nxhi = 2
    devices = mesh.devices.reshape(
        nrow // (nxlo * ncore), nxlo, ncore, nxhi, ncol // nxhi
    )
    fine = Mesh(devices, ("y", "xlo", "core", "xhi", "z"))
    placed = (P(COL, ROW), P(COL, ROW, None), P(), P(), P(), P())
    return jax.shard_map(
        body, mesh=fine, in_specs=placed, out_specs=P(ROW, COL), check_vma=False
    )
```

```python
import jax
import jax.numpy as jnp
from jax import lax
from jax.sharding import Mesh
from jax.sharding import PartitionSpec as P

ROW = ("y", "xlo", "core")
COL = ("xhi", "z")


def lookup(indices, table):
    onehot = (indices[:, None] == jnp.arange(table.shape[0], dtype=jnp.int32)[None, :]).astype(
        jnp.float32
    )
    return jnp.dot(
        onehot, table, precision=lax.Precision.HIGHEST, preferred_element_type=jnp.float32
    )


def split_bf16(x):
    hi = lax.reduce_precision(x, exponent_bits=8, mantissa_bits=7)
    return hi.astype(jnp.bfloat16), (x - hi).astype(jnp.bfloat16)


def body(w_cycle, amps, eps_occ, eps_vir, occ_map, vir_perm):
    nz = lax.axis_size("z")
    nxhi = lax.axis_size("xhi")
    z = lax.axis_index("z")
    xhi = lax.axis_index("xhi")
    col = xhi * nz + z
    row = (lax.axis_index("y") * lax.axis_size("xlo") + lax.axis_index("xlo")) * lax.axis_size(
        "core"
    ) + lax.axis_index("core")

    j_local, b_local, ck = amps.shape
    kw = occ_energy_count = occ_map.shape[0]
    del occ_energy_count
    blk = w_cycle.shape[0]

    vir_energy = lookup(vir_perm, eps_vir)
    occ_energy = lookup(occ_map, eps_occ)
    pair_energy = (vir_energy[None, :] - occ_energy[:, None]).reshape(-1)
    j_index = jnp.arange(j_local, dtype=jnp.int32) + col * j_local
    j_energy = lookup(j_index, eps_occ)
    b_energy = lax.dynamic_slice_in_dim(vir_energy, row * b_local, b_local)
    denominator = pair_energy[None, None, :] + b_energy[None, :, None] - j_energy[:, None, None]
    scaled = amps / denominator

    s5 = scaled.reshape(j_local, b_local, nxhi, nz, blk)
    s5 = jnp.where(xhi == 0, s5, s5[:, :, ::-1])
    s5 = jnp.roll(s5, -z, axis=3)
    s_perm = s5.transpose(0, 1, 3, 2, 4).reshape(j_local, b_local, ck)
    s_full = lax.all_gather(s_perm, ROW, axis=1, tiled=True)
    del kw

    w_other = lax.ppermute(w_cycle, "xhi", [(0, 1), (1, 0)])
    fwd = [(k, (k + 1) % nz) for k in range(nz)]
    bwd = [(k, (k - 1) % nz) for k in range(nz)]
    blocks = {0: [w_cycle, w_other]}
    f_own, f_oth = w_cycle, w_other
    b_own, b_oth = w_cycle, w_other
    half = nz // 2
    for s in range(1, half + 1):
        f_own = lax.ppermute(f_own, "z", fwd)
        b_oth = lax.ppermute(b_oth, "z", bwd)
        if s < half:
            f_oth = lax.ppermute(f_oth, "z", fwd)
            b_own = lax.ppermute(b_own, "z", bwd)
            blocks[nz - s] = [f_own, f_oth]
            blocks[s] = [b_own, b_oth]
        else:
            blocks[s] = [f_own, b_oth]
    s_cols = s_full.reshape(j_local * s_full.shape[1], ck)
    s_hi, s_lo = split_bf16(s_cols)
    width = nxhi * blk
    out = None
    for group in ([0], [1, nz - 1], [2, nz - 2], [3, nz - 3], [half]):
        w_g = jnp.concatenate([blocks[d][t] for d in group for t in range(nxhi)], axis=0)
        w_hi, w_lo = split_bf16(w_g)
        sl = [slice(d * width, (d + 1) * width) for d in group]
        sh_g = jnp.concatenate([s_hi[:, c] for c in sl], axis=1)
        sl_g = jnp.concatenate([s_lo[:, c] for c in sl], axis=1)
        lhs = jnp.concatenate([w_hi, w_hi, w_lo], axis=0)
        rhs = jnp.concatenate([sh_g, sl_g, sh_g], axis=1)
        part = lax.dot_general(
            lhs, rhs, (((0,), (1,)), ((), ())), preferred_element_type=jnp.float32
        )
        out = part if out is None else out + part
    return out


def solution(mesh):
    nrow, ncol = mesh.devices.shape
    ncore = 2
    nxlo = 2
    nxhi = 2
    devices = mesh.devices.reshape(
        nrow // (nxlo * ncore), nxlo, ncore, nxhi, ncol // nxhi
    )
    fine = Mesh(devices, ("y", "xlo", "core", "xhi", "z"))
    placed = (P(COL, ROW), P(COL, ROW, None), P(), P(), P(), P())
    return jax.shard_map(
        body, mesh=fine, in_specs=placed, out_specs=P(ROW, COL), check_vma=False
    )
```

```python
import jax
import jax.numpy as jnp
from jax import lax
from jax.sharding import Mesh
from jax.sharding import PartitionSpec as P


ROW = ("y", "xlo", "core")
COL = ("xhi", "z")


def lookup(indices, table):
    onehot = (indices[:, None] == jnp.arange(table.shape[0], dtype=jnp.int32)[None, :]).astype(
        jnp.float32
    )
    return jnp.dot(
        onehot, table, precision=lax.Precision.HIGHEST, preferred_element_type=jnp.float32
    )


def split_bf16(x):
    hi = lax.reduce_precision(x, exponent_bits=8, mantissa_bits=7)
    return hi.astype(jnp.bfloat16), (x - hi).astype(jnp.bfloat16)


def layer(w_cycle, amps, eps_occ, eps_vir, occ_map, vir_perm):
    nz = lax.axis_size("z")
    nxhi = lax.axis_size("xhi")
    z = lax.axis_index("z")
    xhi = lax.axis_index("xhi")
    col = xhi * nz + z
    row = (lax.axis_index("y") * lax.axis_size("xlo") + lax.axis_index("xlo")) * lax.axis_size(
        "core"
    ) + lax.axis_index("core")
    j_local, b_local, ck = amps.shape
    blk = w_cycle.shape[0]
    half = nz // 2
    fwd = [(k, (k + 1) % nz) for k in range(nz)]
    bwd = [(k, (k - 1) % nz) for k in range(nz)]

    w_other = lax.ppermute(w_cycle, "xhi", [(0, 1), (1, 0)])
    blocks = {0: [w_cycle, w_other]}
    f_own, f_oth = w_cycle, w_other
    b_own, b_oth = w_cycle, w_other
    for s in range(1, half + 1):
        if s < half:
            f_own = lax.ppermute(f_own, "z", fwd)
            b_own = lax.ppermute(b_own, "z", bwd)
            f_oth = lax.ppermute(f_oth, "z", fwd)
            b_oth = lax.ppermute(b_oth, "z", bwd)
            blocks[nz - s] = [f_own, f_oth]
            blocks[s] = [b_own, b_oth]
        else:
            f_own = lax.ppermute(f_own, "z", fwd)
            b_oth = lax.ppermute(b_oth, "z", bwd)
            blocks[s] = [f_own, b_oth]

    vir_energy = lookup(vir_perm, eps_vir)
    occ_energy = lookup(occ_map, eps_occ)
    pair_energy = (vir_energy[None, :] - occ_energy[:, None]).reshape(-1)
    j_index = jnp.arange(j_local, dtype=jnp.int32) + col * j_local
    j_energy = lookup(j_index, eps_occ)
    b_energy = lax.dynamic_slice_in_dim(vir_energy, row * b_local, b_local)
    denominator = pair_energy[None, None, :] + b_energy[None, :, None] - j_energy[:, None, None]
    scaled = amps / denominator
    s5 = scaled.reshape(j_local, b_local, nxhi, nz, blk)
    s5 = jnp.where(xhi == 0, s5, s5[:, :, ::-1])
    s5 = jnp.roll(s5, -z, axis=3)
    s_perm = s5.transpose(0, 1, 3, 2, 4).reshape(j_local, b_local, ck)
    s_full = lax.all_gather(s_perm, ROW, axis=1, tiled=True)

    s_cols = s_full.reshape(j_local * s_full.shape[1], ck)
    s_hi, s_lo = split_bf16(s_cols)
    width = nxhi * blk
    out = None
    for group in ([0], [1, nz - 1], [2, nz - 2], [3, nz - 3], [half]):
        w_g = jnp.concatenate([blocks[d][t] for d in group for t in range(nxhi)], axis=0)
        w_hi, w_lo = split_bf16(w_g)
        sl = [slice(d * width, (d + 1) * width) for d in group]
        sh_g = jnp.concatenate([s_hi[:, c] for c in sl], axis=1)
        sl_g = jnp.concatenate([s_lo[:, c] for c in sl], axis=1)
        lhs = jnp.concatenate([w_hi, w_hi, w_lo], axis=0)
        rhs = jnp.concatenate([sh_g, sl_g, sh_g], axis=1)
        part = lax.dot_general(
            lhs, rhs, (((0,), (1,)), ((), ())), preferred_element_type=jnp.float32
        )
        out = part if out is None else out + part
    return out


def solution(mesh):
    nrow, ncol = mesh.devices.shape
    ncore = 2
    nxlo = 2
    nxhi = 2
    devices = mesh.devices.reshape(
        nrow // (nxlo * ncore), nxlo, ncore, nxhi, ncol // nxhi
    )
    fine = Mesh(devices, ("y", "xlo", "core", "xhi", "z"))
    placed = (P(COL, ROW), P(COL, ROW, None), P(), P(), P(), P())
    return jax.shard_map(layer, mesh=fine, in_specs=placed, out_specs=P(ROW, COL), check_vma=False)
```

```python
import jax
import jax.numpy as jnp
from jax import lax
from jax.sharding import Mesh
from jax.sharding import PartitionSpec as P


ROW = ("y", "xlo", "core")
COL = ("xhi", "z")


def lookup(indices, table):
    onehot = (indices[:, None] == jnp.arange(table.shape[0], dtype=jnp.int32)[None, :]).astype(
        jnp.float32
    )
    return jnp.dot(
        onehot, table, precision=lax.Precision.HIGHEST, preferred_element_type=jnp.float32
    )


def split_bf16(x):
    hi = lax.reduce_precision(x, exponent_bits=8, mantissa_bits=7)
    return hi.astype(jnp.bfloat16), (x - hi).astype(jnp.bfloat16)


def layer(w_cycle, amps, eps_occ, eps_vir, occ_map, vir_perm):
    nz = lax.axis_size("z")
    nxhi = lax.axis_size("xhi")
    z = lax.axis_index("z")
    xhi = lax.axis_index("xhi")
    col = xhi * nz + z
    row = (lax.axis_index("y") * lax.axis_size("xlo") + lax.axis_index("xlo")) * lax.axis_size(
        "core"
    ) + lax.axis_index("core")
    j_local, b_local, ck = amps.shape
    blk = w_cycle.shape[0]
    half = nz // 2
    fwd = [(k, (k + 1) % nz) for k in range(nz)]
    bwd = [(k, (k - 1) % nz) for k in range(nz)]

    w_other = lax.ppermute(w_cycle, "xhi", [(0, 1), (1, 0)])
    blocks = {0: [w_cycle, w_other]}
    f_own, f_oth = w_cycle, w_other
    b_own, b_oth = w_cycle, w_other
    for s in range(1, half + 1):
        if s < half:
            f_own = lax.ppermute(f_own, "z", fwd)
            b_own = lax.ppermute(b_own, "z", bwd)
            f_oth = lax.ppermute(f_oth, "z", fwd)
            b_oth = lax.ppermute(b_oth, "z", bwd)
            blocks[nz - s] = [f_own, f_oth]
            blocks[s] = [b_own, b_oth]
        else:
            f_own = lax.ppermute(f_own, "z", fwd)
            b_oth = lax.ppermute(b_oth, "z", bwd)
            blocks[s] = [f_own, b_oth]

    vir_energy = lookup(vir_perm, eps_vir)
    occ_energy = lookup(occ_map, eps_occ)
    pair_energy = (vir_energy[None, :] - occ_energy[:, None]).reshape(-1)
    j_index = jnp.arange(j_local, dtype=jnp.int32) + col * j_local
    j_energy = lookup(j_index, eps_occ)
    b_energy = lax.dynamic_slice_in_dim(vir_energy, row * b_local, b_local)
    denominator = pair_energy[None, None, :] + b_energy[None, :, None] - j_energy[:, None, None]
    scaled = amps / denominator
    s_full = lax.all_gather(scaled, ROW, axis=1, tiled=True)

    s_cols = s_full.reshape(j_local * s_full.shape[1], ck)
    s_hi, s_lo = split_bf16(s_cols)
    out = None
    for group in ([0], [1, nz - 1], [2, nz - 2], [3, nz - 3], [half]):
        w_g = jnp.concatenate([blocks[d][t] for d in group for t in range(nxhi)], axis=0)
        w_hi, w_lo = split_bf16(w_g)
        starts = [((xhi + t) % nxhi * nz + (z + d) % nz) * blk for d in group for t in range(nxhi)]
        sh_g = jnp.concatenate([lax.dynamic_slice_in_dim(s_hi, c, blk, 1) for c in starts], 1)
        sl_g = jnp.concatenate([lax.dynamic_slice_in_dim(s_lo, c, blk, 1) for c in starts], 1)
        lhs = jnp.concatenate([w_hi, w_hi, w_lo], axis=0)
        rhs = jnp.concatenate([sh_g, sl_g, sh_g], axis=1)
        part = lax.dot_general(
            lhs, rhs, (((0,), (1,)), ((), ())), preferred_element_type=jnp.float32
        )
        if out is None:
            out = part
        else:
            out = out + part
    return out


def solution(mesh):
    nrow, ncol = mesh.devices.shape
    ncore = 2
    nxlo = 2
    nxhi = 2
    devices = mesh.devices.reshape(
        nrow // (nxlo * ncore), nxlo, ncore, nxhi, ncol // nxhi
    )
    fine = Mesh(devices, ("y", "xlo", "core", "xhi", "z"))
    placed = (P(COL, ROW), P(COL, ROW, None), P(), P(), P(), P())
    return jax.shard_map(layer, mesh=fine, in_specs=placed, out_specs=P(ROW, COL), check_vma=False)
```

```python
import jax
import jax.numpy as jnp
from jax import lax
from jax.sharding import Mesh
from jax.sharding import PartitionSpec as P


ROW = ("y", "xlo", "core")
COL = ("xhi", "z")


def lookup(indices, table):
    onehot = (indices[:, None] == jnp.arange(table.shape[0], dtype=jnp.int32)[None, :]).astype(
        jnp.float32
    )
    return jnp.dot(
        onehot, table, precision=lax.Precision.HIGHEST, preferred_element_type=jnp.float32
    )


def split_bf16(x):
    hi = lax.reduce_precision(x, exponent_bits=8, mantissa_bits=7)
    return hi.astype(jnp.bfloat16), (x - hi).astype(jnp.bfloat16)


def layer(w_cycle, amps, eps_occ, eps_vir, occ_map, vir_perm):
    nz = lax.axis_size("z")
    nxhi = lax.axis_size("xhi")
    z = lax.axis_index("z")
    xhi = lax.axis_index("xhi")
    col = xhi * nz + z
    row = (lax.axis_index("y") * lax.axis_size("xlo") + lax.axis_index("xlo")) * lax.axis_size(
        "core"
    ) + lax.axis_index("core")
    j_local, b_local, ck = amps.shape
    blk = w_cycle.shape[0]
    half = nz // 2
    fwd = [(k, (k + 1) % nz) for k in range(nz)]
    bwd = [(k, (k - 1) % nz) for k in range(nz)]

    w_other = lax.ppermute(w_cycle, "xhi", [(0, 1), (1, 0)])
    blocks = {0: [w_cycle, w_other]}
    f_own, f_oth = w_cycle, w_other
    b_own, b_oth = w_cycle, w_other
    for s in range(1, half + 1):
        if s < half:
            f_own = lax.ppermute(f_own, "z", fwd)
            b_own = lax.ppermute(b_own, "z", bwd)
            f_oth = lax.ppermute(f_oth, "z", fwd)
            b_oth = lax.ppermute(b_oth, "z", bwd)
            blocks[nz - s] = [f_own, f_oth]
            blocks[s] = [b_own, b_oth]
        else:
            f_own = lax.ppermute(f_own, "z", fwd)
            b_oth = lax.ppermute(b_oth, "z", bwd)
            blocks[s] = [f_own, b_oth]

    vir_energy = lookup(vir_perm, eps_vir)
    occ_energy = lookup(occ_map, eps_occ)
    pair_energy = (vir_energy[None, :] - occ_energy[:, None]).reshape(-1)
    j_index = jnp.arange(j_local, dtype=jnp.int32) + col * j_local
    j_energy = lookup(j_index, eps_occ)
    b_energy = lax.dynamic_slice_in_dim(vir_energy, row * b_local, b_local)
    denominator = pair_energy[None, None, :] + b_energy[None, :, None] - j_energy[:, None, None]
    scaled = amps / denominator
    s5 = scaled.reshape(j_local, b_local, nxhi, nz, blk)
    s5 = jnp.where(xhi == 0, s5, s5[:, :, ::-1])
    s5 = jnp.roll(s5, -z, axis=3)
    s_perm = s5.transpose(0, 1, 3, 2, 4).reshape(j_local, b_local, ck)
    s_full = lax.all_gather(s_perm, ROW, axis=1, tiled=True)

    s_cols = s_full.reshape(j_local * s_full.shape[1], ck)
    s_hi, s_lo = split_bf16(s_cols)
    width = nxhi * blk
    out = None
    for group in ([0], [1, nz - 1], [2, nz - 2], [3, nz - 3], [half]):
        w_g = jnp.concatenate([blocks[d][t] for d in group for t in range(nxhi)], axis=0)
        w_hi, w_lo = split_bf16(w_g)
        lhs = jnp.concatenate([w_hi, w_hi, w_lo], axis=0)
        sl = [slice(d * width, (d + 1) * width) for d in group]
        sh_g = jnp.concatenate([s_hi[:, c] for c in sl], axis=1)
        sl_g = jnp.concatenate([s_lo[:, c] for c in sl], axis=1)
        rhs = jnp.concatenate([sh_g, sl_g, sh_g], axis=1)
        part = lax.dot_general(
            lhs, rhs, (((0,), (1,)), ((), ())), preferred_element_type=jnp.float32
        )
        if out is None:
            out = part
        else:
            out = out + part
    return out


def solution(mesh):
    nrow, ncol = mesh.devices.shape
    ncore = 2
    nxlo = 2
    nxhi = 2
    devices = mesh.devices.reshape(
        nrow // (nxlo * ncore), nxlo, ncore, nxhi, ncol // nxhi
    )
    fine = Mesh(devices, ("y", "xlo", "core", "xhi", "z"))
    placed = (P(COL, ROW), P(COL, ROW, None), P(), P(), P(), P())
    return jax.shard_map(layer, mesh=fine, in_specs=placed, out_specs=P(ROW, COL), check_vma=False)
```

```python
import jax
import jax.numpy as jnp
from jax import lax
from jax.sharding import Mesh
from jax.sharding import PartitionSpec as P


ROW = ("y", "xlo", "core")
COL = ("xhi", "z")


def lookup(indices, table):
    onehot = (indices[:, None] == jnp.arange(table.shape[0], dtype=jnp.int32)[None, :]).astype(
        jnp.float32
    )
    return jnp.dot(
        onehot, table, precision=lax.Precision.HIGHEST, preferred_element_type=jnp.float32
    )


def split_bf16(x):
    hi = lax.reduce_precision(x, exponent_bits=8, mantissa_bits=7)
    return hi.astype(jnp.bfloat16), (x - hi).astype(jnp.bfloat16)


def layer(w_cycle, amps, eps_occ, eps_vir, occ_map, vir_perm):
    nz = lax.axis_size("z")
    nxhi = lax.axis_size("xhi")
    z = lax.axis_index("z")
    xhi = lax.axis_index("xhi")
    col = xhi * nz + z
    row = (lax.axis_index("y") * lax.axis_size("xlo") + lax.axis_index("xlo")) * lax.axis_size(
        "core"
    ) + lax.axis_index("core")
    j_local, b_local, ck = amps.shape
    blk = w_cycle.shape[0]
    half = nz // 2
    fwd = [(k, (k + 1) % nz) for k in range(nz)]
    bwd = [(k, (k - 1) % nz) for k in range(nz)]

    w_other = lax.ppermute(w_cycle, "xhi", [(0, 1), (1, 0)])
    blocks = {0: [w_cycle, w_other]}
    f_own, f_oth = w_cycle, w_other
    b_own, b_oth = w_cycle, w_other
    for s in range(1, half + 1):
        if s < half:
            f_own = lax.ppermute(f_own, "z", fwd)
            b_own = lax.ppermute(b_own, "z", bwd)
            f_oth = lax.ppermute(f_oth, "z", fwd)
            b_oth = lax.ppermute(b_oth, "z", bwd)
            blocks[nz - s] = [f_own, f_oth]
            blocks[s] = [b_own, b_oth]
        else:
            f_own = lax.ppermute(f_own, "z", fwd)
            b_oth = lax.ppermute(b_oth, "z", bwd)
            blocks[s] = [f_own, b_oth]

    vir_energy = lookup(vir_perm, eps_vir)
    occ_energy = lookup(occ_map, eps_occ)
    pair_energy = (vir_energy[None, :] - occ_energy[:, None]).reshape(-1)
    j_energy = lax.dynamic_slice_in_dim(eps_occ, col * j_local, j_local)
    b_energy = lax.dynamic_slice_in_dim(vir_energy, row * b_local, b_local)
    denominator = pair_energy[None, None, :] + b_energy[None, :, None] - j_energy[:, None, None]
    scaled = amps / denominator
    s5 = scaled.reshape(j_local, b_local, nxhi, nz, blk)
    s5 = jnp.where(xhi == 0, s5, s5[:, :, ::-1])
    s5 = jnp.roll(s5, -z, axis=3)
    s_perm = s5.transpose(0, 1, 3, 2, 4).reshape(j_local, b_local, ck)
    core = lax.axis_index("core")
    swap = [(0, 1), (1, 0)]
    s_sib = lax.ppermute(s_perm, "core", swap)
    half_j = jnp.where(
        core == 0,
        jnp.concatenate([s_perm[0:1], s_sib[0:1]], axis=1),
        jnp.concatenate([s_sib[1:2], s_perm[1:2]], axis=1),
    )
    s_mine = lax.all_gather(half_j, ("y", "xlo"), axis=1, tiled=True)
    s_other = lax.ppermute(s_mine, "core", swap)

    s_full = jnp.where(
        core == 0,
        jnp.concatenate([s_mine, s_other], axis=0),
        jnp.concatenate([s_other, s_mine], axis=0),
    )
    s_cols = s_full.reshape(j_local * s_full.shape[1], ck)
    s_hi, s_lo = split_bf16(s_cols)
    width = nxhi * blk
    out = None
    for group in ([0], [1, nz - 1], [2, nz - 2], [3, nz - 3], [half]):
        w_g = jnp.concatenate([blocks[d][t] for d in group for t in range(nxhi)], axis=0)
        w_hi, w_lo = split_bf16(w_g)
        lhs = jnp.concatenate([w_hi, w_hi, w_lo], axis=0)
        sl = [slice(d * width, (d + 1) * width) for d in group]
        sh_g = jnp.concatenate([s_hi[:, c] for c in sl], axis=1)
        sl_g = jnp.concatenate([s_lo[:, c] for c in sl], axis=1)
        rhs = jnp.concatenate([sh_g, sl_g, sh_g], axis=1)
        part = lax.dot_general(
            lhs, rhs, (((0,), (1,)), ((), ())), preferred_element_type=jnp.float32
        )
        if out is None:
            out = part
        else:
            out = out + part
    return out


def solution(mesh):
    nrow, ncol = mesh.devices.shape
    ncore = 2
    nxlo = 2
    nxhi = 2
    devices = mesh.devices.reshape(
        nrow // (nxlo * ncore), nxlo, ncore, nxhi, ncol // nxhi
    )
    fine = Mesh(devices, ("y", "xlo", "core", "xhi", "z"))
    placed = (P(COL, ROW), P(COL, ROW, None), P(), P(), P(), P())
    return jax.shard_map(layer, mesh=fine, in_specs=placed, out_specs=P(ROW, COL), check_vma=False)
```

```python
import jax
import jax.numpy as jnp
from jax import lax
from jax.sharding import Mesh
from jax.sharding import PartitionSpec as P


ROW = ("y", "xlo", "core")
COL = ("xhi", "z")
ARRIVAL = (0, 1, 7, 2, 6, 3, 5, 4)


def lookup(indices, table):
    onehot = (indices[:, None] == jnp.arange(table.shape[0], dtype=jnp.int32)[None, :]).astype(
        jnp.float32
    )
    return jnp.dot(
        onehot, table, precision=lax.Precision.HIGHEST, preferred_element_type=jnp.float32
    )


def split_bf16(x):
    hi = lax.reduce_precision(x, exponent_bits=8, mantissa_bits=7)
    return hi.astype(jnp.bfloat16), (x - hi).astype(jnp.bfloat16)


def layer(w_cycle, amps, eps_occ, eps_vir, occ_map, vir_perm):
    nz = lax.axis_size("z")
    nxhi = lax.axis_size("xhi")
    z = lax.axis_index("z")
    xhi = lax.axis_index("xhi")
    col = xhi * nz + z
    row = (lax.axis_index("y") * lax.axis_size("xlo") + lax.axis_index("xlo")) * lax.axis_size(
        "core"
    ) + lax.axis_index("core")
    j_local, b_local, ck = amps.shape
    blk = w_cycle.shape[0]
    half = nz // 2
    fwd = [(k, (k + 1) % nz) for k in range(nz)]
    bwd = [(k, (k - 1) % nz) for k in range(nz)]

    w_other = lax.ppermute(w_cycle, "xhi", [(0, 1), (1, 0)])
    blocks = {0: [w_cycle, w_other]}
    f_own, f_oth = w_cycle, w_other
    b_own, b_oth = w_cycle, w_other
    for s in range(1, half + 1):
        if s < half:
            f_own = lax.ppermute(f_own, "z", fwd)
            b_own = lax.ppermute(b_own, "z", bwd)
            f_oth = lax.ppermute(f_oth, "z", fwd)
            b_oth = lax.ppermute(b_oth, "z", bwd)
            blocks[nz - s] = [f_own, f_oth]
            blocks[s] = [b_own, b_oth]
        else:
            f_own = lax.ppermute(f_own, "z", fwd)
            b_oth = lax.ppermute(b_oth, "z", bwd)
            blocks[s] = [f_own, b_oth]

    vir_energy = lookup(vir_perm, eps_vir)
    occ_energy = lookup(occ_map, eps_occ)
    pair_energy = (vir_energy[None, :] - occ_energy[:, None]).reshape(-1)
    j_energy = lax.dynamic_slice_in_dim(eps_occ, col * j_local, j_local)
    b_energy = lax.dynamic_slice_in_dim(vir_energy, row * b_local, b_local)
    denominator = pair_energy[None, None, :] + b_energy[None, :, None] - j_energy[:, None, None]
    scaled = amps / denominator
    s5 = scaled.reshape(j_local, b_local, nxhi, nz, blk)
    s5 = jnp.where(xhi == 0, s5, s5[:, :, ::-1])
    s5 = jnp.roll(s5, -z, axis=3)
    s5 = jnp.concatenate([s5[:, :, :, d : d + 1] for d in ARRIVAL], axis=3)
    s_perm = s5.transpose(0, 1, 3, 2, 4).reshape(j_local, b_local, ck)
    s_early = lax.all_gather(s_perm[:, :, : ck // 2], ROW, axis=1, tiled=True)
    s_late = lax.all_gather(s_perm[:, :, ck // 2 :], ROW, axis=1, tiled=True)

    rows = j_local * s_early.shape[1]
    s_hi_a, s_lo_a = split_bf16(s_early.reshape(rows, ck // 2))
    s_hi_b, s_lo_b = split_bf16(s_late.reshape(rows, ck // 2))
    width = nxhi * blk
    per_half = nz // 2
    where_of = {d: k for k, d in enumerate(ARRIVAL)}

    def s_block(d, hi):
        k = where_of[d]
        src = (s_hi_a if hi else s_lo_a) if k < per_half else (s_hi_b if hi else s_lo_b)
        k = k % per_half
        return src[:, k * width : (k + 1) * width]
    out = None
    for group in ([0], [1, nz - 1], [2, nz - 2], [3, nz - 3], [half]):
        w_g = jnp.concatenate([blocks[d][t] for d in group for t in range(nxhi)], axis=0)
        w_hi, w_lo = split_bf16(w_g)
        lhs = jnp.concatenate([w_hi, w_hi, w_lo], axis=0)
        sh_g = jnp.concatenate([s_block(d, True) for d in group], axis=1)
        sl_g = jnp.concatenate([s_block(d, False) for d in group], axis=1)
        rhs = jnp.concatenate([sh_g, sl_g, sh_g], axis=1)
        part = lax.dot_general(
            lhs, rhs, (((0,), (1,)), ((), ())), preferred_element_type=jnp.float32
        )
        if out is None:
            out = part
        else:
            out = out + part
    return out


def solution(mesh):
    nrow, ncol = mesh.devices.shape
    ncore = 2
    nxlo = 2
    nxhi = 2
    devices = mesh.devices.reshape(
        nrow // (nxlo * ncore), nxlo, ncore, nxhi, ncol // nxhi
    )
    fine = Mesh(devices, ("y", "xlo", "core", "xhi", "z"))
    placed = (P(COL, ROW), P(COL, ROW, None), P(), P(), P(), P())
    return jax.shard_map(layer, mesh=fine, in_specs=placed, out_specs=P(ROW, COL), check_vma=False)
```

```python
import jax
import jax.numpy as jnp
from jax import lax
from jax.sharding import Mesh
from jax.sharding import PartitionSpec as P


ROW = ("y", "xlo", "core")
COL = ("xhi", "z")


def lookup(indices, table):
    onehot = (indices[:, None] == jnp.arange(table.shape[0], dtype=jnp.int32)[None, :]).astype(
        jnp.float32
    )
    return jnp.dot(
        onehot, table, precision=lax.Precision.HIGHEST, preferred_element_type=jnp.float32
    )


def split_bf16(x):
    hi = lax.reduce_precision(x, exponent_bits=8, mantissa_bits=7)
    return hi.astype(jnp.bfloat16), (x - hi).astype(jnp.bfloat16)


def layer(w_cycle, amps, eps_occ, eps_vir, occ_map, vir_perm):
    nz = lax.axis_size("z")
    nxhi = lax.axis_size("xhi")
    z = lax.axis_index("z")
    xhi = lax.axis_index("xhi")
    col = xhi * nz + z
    row = (lax.axis_index("y") * lax.axis_size("xlo") + lax.axis_index("xlo")) * lax.axis_size(
        "core"
    ) + lax.axis_index("core")
    j_local, b_local, ck = amps.shape
    blk = w_cycle.shape[0]
    half = nz // 2
    fwd = [(k, (k + 1) % nz) for k in range(nz)]
    bwd = [(k, (k - 1) % nz) for k in range(nz)]

    w_other = lax.ppermute(w_cycle, "xhi", [(0, 1), (1, 0)])
    blocks = {0: [w_cycle, w_other]}
    f_own, f_oth = w_cycle, w_other
    b_own, b_oth = w_cycle, w_other
    for s in range(1, half + 1):
        if s < half:
            f_own = lax.ppermute(f_own, "z", fwd)
            b_own = lax.ppermute(b_own, "z", bwd)
            f_oth = lax.ppermute(f_oth, "z", fwd)
            b_oth = lax.ppermute(b_oth, "z", bwd)
            blocks[nz - s] = [f_own, f_oth]
            blocks[s] = [b_own, b_oth]
        else:
            f_own = lax.ppermute(f_own, "z", fwd)
            b_oth = lax.ppermute(b_oth, "z", bwd)
            blocks[s] = [f_own, b_oth]

    vir_energy = lookup(vir_perm, eps_vir)
    occ_energy = lookup(occ_map, eps_occ)
    pair_energy = (vir_energy[None, :] - occ_energy[:, None]).reshape(-1)
    j_energy = lax.dynamic_slice_in_dim(eps_occ, col * j_local, j_local)
    b_energy = lax.dynamic_slice_in_dim(vir_energy, row * b_local, b_local)
    denominator = pair_energy[None, None, :] + b_energy[None, :, None] - j_energy[:, None, None]
    scaled = amps / denominator
    s5 = scaled.reshape(j_local, b_local, nxhi, nz, blk)
    s5 = jnp.where(xhi == 0, s5, s5[:, :, ::-1])
    s5 = jnp.roll(s5, -z, axis=3)
    s_perm = s5.transpose(0, 1, 3, 2, 4).reshape(j_local, b_local, ck)
    s_rows = lax.all_gather(s_perm.reshape(j_local * b_local, ck), ROW, axis=0, tiled=True)

    nrow = s_rows.shape[0] // (j_local * b_local)
    s_cols = (
        s_rows.reshape(nrow, j_local, b_local, ck)
        .transpose(1, 0, 2, 3)
        .reshape(nrow * j_local * b_local, ck)
    )
    s_hi, s_lo = split_bf16(s_cols)
    width = nxhi * blk
    out = None
    for group in ([0], [1, nz - 1], [2, nz - 2], [3, nz - 3], [half]):
        w_g = jnp.concatenate([blocks[d][t] for d in group for t in range(nxhi)], axis=0)
        w_hi, w_lo = split_bf16(w_g)
        lhs = jnp.concatenate([w_hi, w_hi, w_lo], axis=0)
        sl = [slice(d * width, (d + 1) * width) for d in group]
        sh_g = jnp.concatenate([s_hi[:, c] for c in sl], axis=1)
        sl_g = jnp.concatenate([s_lo[:, c] for c in sl], axis=1)
        rhs = jnp.concatenate([sh_g, sl_g, sh_g], axis=1)
        part = lax.dot_general(
            lhs, rhs, (((0,), (1,)), ((), ())), preferred_element_type=jnp.float32
        )
        if out is None:
            out = part
        else:
            out = out + part
    return out


def solution(mesh):
    nrow, ncol = mesh.devices.shape
    ncore = 2
    nxlo = 2
    nxhi = 2
    devices = mesh.devices.reshape(
        nrow // (nxlo * ncore), nxlo, ncore, nxhi, ncol // nxhi
    )
    fine = Mesh(devices, ("y", "xlo", "core", "xhi", "z"))
    placed = (P(COL, ROW), P(COL, ROW, None), P(), P(), P(), P())
    return jax.shard_map(layer, mesh=fine, in_specs=placed, out_specs=P(ROW, COL), check_vma=False)
```

```python
import jax
import jax.numpy as jnp
from jax import lax
from jax.sharding import Mesh
from jax.sharding import PartitionSpec as P


ROW = ("y", "xlo", "core")
COL = ("xhi", "z")


def lookup(indices, table):
    onehot = (indices[:, None] == jnp.arange(table.shape[0], dtype=jnp.int32)[None, :]).astype(
        jnp.float32
    )
    return jnp.dot(
        onehot, table, precision=lax.Precision.HIGHEST, preferred_element_type=jnp.float32
    )


def split_bf16(x):
    hi = lax.reduce_precision(x, exponent_bits=8, mantissa_bits=7)
    return hi.astype(jnp.bfloat16), (x - hi).astype(jnp.bfloat16)


def layer(w_cycle, amps, eps_occ, eps_vir, occ_map, vir_perm):
    nz = lax.axis_size("z")
    nxhi = lax.axis_size("xhi")
    z = lax.axis_index("z")
    xhi = lax.axis_index("xhi")
    col = xhi * nz + z
    row = (lax.axis_index("y") * lax.axis_size("xlo") + lax.axis_index("xlo")) * lax.axis_size(
        "core"
    ) + lax.axis_index("core")
    j_local, b_local, ck = amps.shape
    blk = w_cycle.shape[0]
    half = nz // 2
    fwd = [(k, (k + 1) % nz) for k in range(nz)]
    bwd = [(k, (k - 1) % nz) for k in range(nz)]

    w_other = lax.ppermute(w_cycle, "xhi", [(0, 1), (1, 0)])
    blocks = {0: [w_cycle, w_other]}
    f_own, f_oth = w_cycle, w_other
    b_own, b_oth = w_cycle, w_other
    for s in range(1, half + 1):
        if s < half:
            f_own = lax.ppermute(f_own, "z", fwd)
            b_own = lax.ppermute(b_own, "z", bwd)
            f_oth = lax.ppermute(f_oth, "z", fwd)
            b_oth = lax.ppermute(b_oth, "z", bwd)
            blocks[nz - s] = [f_own, f_oth]
            blocks[s] = [b_own, b_oth]
        else:
            f_own = lax.ppermute(f_own, "z", fwd)
            b_oth = lax.ppermute(b_oth, "z", bwd)
            blocks[s] = [f_own, b_oth]

    vir_energy = lookup(vir_perm, eps_vir)
    occ_energy = lookup(occ_map, eps_occ)
    pair_energy = (vir_energy[None, :] - occ_energy[:, None]).reshape(-1)
    j_energy = lax.dynamic_slice_in_dim(eps_occ, col * j_local, j_local)
    b_energy = lax.dynamic_slice_in_dim(vir_energy, row * b_local, b_local)
    denominator = pair_energy[None, None, :] + b_energy[None, :, None] - j_energy[:, None, None]
    scaled = amps / denominator
    s5 = scaled.reshape(j_local, b_local, nxhi, nz, blk)
    s5 = jnp.where(xhi == 0, s5, s5[:, :, ::-1])
    s5 = jnp.roll(s5, -z, axis=3)
    s_perm = s5.transpose(0, 1, 3, 2, 4).reshape(j_local, b_local, ck)
    s_full = lax.all_gather(s_perm, ROW, axis=1, tiled=True)

    s_cols = s_full.reshape(j_local * s_full.shape[1], ck)
    s_hi, s_lo = split_bf16(s_cols)
    width = nxhi * blk
    out = None
    for group in ([0], [1, nz - 1], [2, nz - 2], [3, nz - 3, half]):
        w_g = jnp.concatenate([blocks[d][t] for d in group for t in range(nxhi)], axis=0)
        w_hi, w_lo = split_bf16(w_g)
        lhs = jnp.concatenate([w_hi, w_hi, w_lo], axis=0)
        sl = [slice(d * width, (d + 1) * width) for d in group]
        sh_g = jnp.concatenate([s_hi[:, c] for c in sl], axis=1)
        sl_g = jnp.concatenate([s_lo[:, c] for c in sl], axis=1)
        rhs = jnp.concatenate([sh_g, sl_g, sh_g], axis=1)
        part = lax.dot_general(
            lhs, rhs, (((0,), (1,)), ((), ())), preferred_element_type=jnp.float32
        )
        if out is None:
            out = part
        else:
            out = out + part
    return out


def solution(mesh):
    nrow, ncol = mesh.devices.shape
    ncore = 2
    nxlo = 2
    nxhi = 2
    devices = mesh.devices.reshape(
        nrow // (nxlo * ncore), nxlo, ncore, nxhi, ncol // nxhi
    )
    fine = Mesh(devices, ("y", "xlo", "core", "xhi", "z"))
    placed = (P(COL, ROW), P(COL, ROW, None), P(), P(), P(), P())
    return jax.shard_map(layer, mesh=fine, in_specs=placed, out_specs=P(ROW, COL), check_vma=False)
```
